512 devices in a mesh: tm: 32 (over y, x), rows: 16 (over z, core).
Axes of the slice: x: 4, y: 8, z: 8, core: 2. Of those that a mesh axis runs over, the one named last changes fastest.
Arguments:
- features: bfloat16 [64, 16, 40, 384], P('tm', 'rows'), may hold values from -6 to 6
- gain_one: float32 [384], replicated, may hold values from 0.1 to 1.9
- weight_one: bfloat16 [384, 3, 3, 3, 384], P('rows'), may hold values from -0.0625 to 0.0625
- bias_one: float32 [384], replicated, may hold values from -3 to 3
- gain_two: float32 [384], replicated, may hold values from 0.1 to 1.9
- weight_two: bfloat16 [384, 3, 3, 3, 384], P('rows'), may hold values from -0.0625 to 0.0625
- bias_two: float32 [384], replicated, may hold values from -3 to 3
Outputs:
- block_out: bfloat16 [64, 16, 40, 384], P('tm', 'rows')
The draws below stay inside these ranges and needn't reach their ends.
All inputs are finite; a program needn't handle non-finite values.
Results may differ from the reference program's by a relative error of at most 0.0049.
Values may be sent and summed in bfloat16 or wider, within the bound.
No kernel may reach another device: no remote copies, remote signals or barrier semaphores. Data moves between devices by JAX's collectives and lax.ppermute only.
A program may use at most 64 MiB of HBM per device.

```python
import jax
import jax.numpy as jnp
from jax import lax

C = 384
WIDTH = 40
FRAMES = 64
HEIGHT = 16


def levels(key, extent, shards, low, largest):
    level = 1.0
    for axis_at, parts in shards:
        steps = jax.random.uniform(jax.random.fold_in(jax.random.fold_in(key, 6), axis_at), (parts,), jnp.float32, low / len(shards), largest / len(shards))
        level = level * jnp.repeat(jnp.exp(steps), extent[axis_at] // parts).reshape((-1,) + (1,) * (len(extent) - 1 - axis_at))
    return level


def noise(own_key, dims, deviation, limit, split=(), held_as=jnp.bfloat16):
    drawn = deviation * jax.random.normal(own_key, dims, jnp.float32)
    if split:
        drawn = drawn * levels(own_key, dims, split, -0.22, 0.18)
    return jnp.clip(drawn, -limit, limit).astype(held_as)


def setup_inputs(seed: int = 0) -> dict:
    seeds = jax.random.split(jax.random.key(seed), 8)
    features = noise(seeds[0], (FRAMES, HEIGHT, WIDTH, C), 1.0, 6.0, ((0, 32), (1, 16)))
    gain_one = jnp.clip(1.0 + 0.18 * jax.random.normal(seeds[1], (C,), jnp.float32), 0.1, 1.9)
    weight_one = noise(seeds[2], (C, 3, 3, 3, C), (27 * C) ** -0.5, 0.0625, ((0, 16),))
    bias_one = noise(seeds[3], (C,), 0.5, 3.0, (), jnp.float32)
    gain_two = jnp.clip(1.0 + 0.18 * jax.random.normal(seeds[4], (C,), jnp.float32), 0.1, 1.9)
    weight_two = noise(seeds[5], (C, 3, 3, 3, C), (27 * C) ** -0.5, 0.0625, ((0, 16),))
    bias_two = noise(seeds[6], (C,), 0.5, 3.0, (), jnp.float32)
    return dict(features=features, gain_one=gain_one, weight_one=weight_one, bias_one=bias_one, gain_two=gain_two, weight_two=weight_two, bias_two=bias_two)


def norm_silu(values, norm_gain):
    values = values.astype(jnp.float32)
    mean_square = lax.optimization_barrier(jnp.mean(values * values, axis=-1, keepdims=True))
    scaled = values * lax.rsqrt(mean_square + 1e-06) * norm_gain.astype(jnp.float32)
    return jax.nn.silu(scaled).astype(jnp.bfloat16)

def causal_conv(inputs, kernel, bias_vec):
    height = inputs.shape[1]
    columns = inputs.shape[2]
    channels = inputs.shape[3]
    outputs = kernel.shape[0]
    padded = jnp.pad(inputs, ((2, 0), (1, 1), (1, 1), (0, 0)))

    def frame_out(frame):
        window = lax.dynamic_slice_in_dim(padded, frame, 3, 0)
        summed = jnp.zeros((height * columns, outputs), jnp.float32)
        for tap_time in range(3):
            for tap_row in range(3):
                for tap_col in range(3):
                    sliced = window[tap_time, tap_row:tap_row + height, tap_col:tap_col + columns, :]
                    summed = summed + jnp.dot(sliced.reshape(height * columns, channels), kernel[:, tap_time, tap_row, tap_col, :].T, preferred_element_type=jnp.float32)
        return summed.reshape(height, columns, outputs) + bias_vec.astype(jnp.float32)
    return lax.map(frame_out, jnp.arange(inputs.shape[0], dtype=jnp.int32))

def reference(features, gain_one, weight_one, bias_one, gain_two, weight_two, bias_two):
    normed_one = norm_silu(features, gain_one)
    conv_one = causal_conv(normed_one, weight_one, bias_one).astype(jnp.bfloat16)
    normed_two = norm_silu(conv_one, gain_two)
    conv_two = causal_conv(normed_two, weight_two, bias_two)
    return (features.astype(jnp.float32) + conv_two).astype(jnp.bfloat16)
```

```python
import jax
import jax.numpy as jnp
from jax import lax
from jax.sharding import Mesh, PartitionSpec as P

CORES = 2


def passed_along(x, axis, by):
    peers = lax.axis_size(axis)
    pairs = [(i, i + by) for i in range(peers) if 0 <= i + by < peers]
    return lax.ppermute(x, axis, pairs)


def norm_silu(values, norm_gain):
    values = values.astype(jnp.float32)
    mean_square = jnp.mean(values * values, axis=-1, keepdims=True)
    scaled = values * lax.rsqrt(mean_square + 1e-06) * norm_gain
    return jax.nn.silu(scaled).astype(jnp.bfloat16)


def gather_rows(x):
    frames, _, columns, channels = x.shape
    along_z = lax.all_gather(x, "z", axis=1, tiled=True)
    both = lax.all_gather(along_z, "core", axis=2, tiled=False)
    return both.reshape(frames, -1, columns, channels)


def scatter_rows(y):
    frames, rows, columns, part_width = y.shape
    y = y.reshape(frames, rows // CORES, CORES, columns, part_width)
    y = lax.all_to_all(y, "z", split_axis=1, concat_axis=1, tiled=True)
    y = lax.all_to_all(y, "core", split_axis=2, concat_axis=2, tiled=True)
    y = jnp.transpose(y, (0, 3, 1, 2, 4))
    return y.reshape(frames, 1, columns, rows * part_width)


def causal_conv(extended, kernel, bias_part):
    out = lax.conv_general_dilated(
        extended[None],
        kernel,
        window_strides=(1, 1, 1),
        padding=((0, 0), (1, 1), (1, 1)),
        dimension_numbers=("NDHWC", "ODHWI", "NDHWC"),
        preferred_element_type=jnp.float32,
    )
    return out[0] + bias_part


def shards(features, gain_one, weight_one, bias_one, gain_two, weight_two, bias_two):
    part_width = weight_one.shape[0]
    index = lax.axis_index("z") * CORES + lax.axis_index("core")
    offset = index * part_width
    bias_first = lax.dynamic_slice_in_dim(bias_one, offset, part_width, 0)
    bias_second = lax.dynamic_slice_in_dim(bias_two, offset, part_width, 0)
    normed_one = norm_silu(features, gain_one)
    prior_one = passed_along(normed_one, "tm", 1)
    extended_one = jnp.concatenate([prior_one, normed_one], 0)
    full_one = gather_rows(extended_one)
    conv_one = causal_conv(full_one, weight_one, bias_first).astype(jnp.bfloat16)
    own_rows = scatter_rows(conv_one)
    normed_two = norm_silu(own_rows, gain_two)
    prior_two = passed_along(normed_two, "tm", 1)
    extended_two = jnp.concatenate([prior_two, normed_two], 0)
    full_two = gather_rows(extended_two)
    conv_two = causal_conv(full_two, weight_two, bias_second)
    returned = scatter_rows(conv_two)
    return (features.astype(jnp.float32) + returned).astype(jnp.bfloat16)


def solution(mesh):
    tm = mesh.shape["tm"]
    rows = mesh.shape["rows"]
    split = Mesh(mesh.devices.reshape(tm, rows // CORES, CORES), ("tm", "z", "core"))
    row_axes = ("z", "core")
    in_specs = (
        P("tm", row_axes, None, None),
        P(),
        P(row_axes, None, None, None, None),
        P(),
        P(),
        P(row_axes, None, None, None, None),
        P(),
    )
    out_specs = P("tm", row_axes, None, None)
    return jax.shard_map(shards, mesh=split, in_specs=in_specs, out_specs=out_specs, check_vma=False)
```

```python
import jax
import jax.numpy as jnp
from jax import lax
from jax.sharding import Mesh, PartitionSpec as P

CORES = 2
ROW_AXES = ("z", "core")


def passed_along(x, axis, by):
    peers = lax.axis_size(axis)
    pairs = [(i, i + by) for i in range(peers) if 0 <= i + by < peers]
    return lax.ppermute(x, axis, pairs)


def norm_silu(values, norm_gain):
    values = values.astype(jnp.float32)
    mean_square = jnp.mean(values * values, axis=-1, keepdims=True)
    scaled = values * lax.rsqrt(mean_square + 1e-06) * norm_gain
    return jax.nn.silu(scaled).astype(jnp.bfloat16)


def rotated(stacked, start):
    n = stacked.shape[0]
    doubled = jnp.concatenate([stacked, stacked], 0)
    return lax.dynamic_slice_in_dim(doubled, start, n, 0)


def gather_rows(x):
    n = lax.axis_size("z")
    z = lax.axis_index("z")
    core = lax.axis_index("core")
    forward = [(i, (i + 1) % n) for i in range(n)]
    backward = [(i, (i - 1) % n) for i in range(n)]
    got = {0: x[:, 0]}
    ahead = behind = x[:, 0]
    for step in range(1, n // 2 + 1):
        behind = lax.ppermute(behind, "z", forward)
        got[-step] = behind
        if step < n - step:
            ahead = lax.ppermute(ahead, "z", backward)
            got[step] = ahead
    half = n // 2
    relative = jnp.stack([got[k - half] for k in range(n)], 0)
    mine = rotated(relative, (half - z) % n)
    other = lax.ppermute(mine, "core", [(0, 1), (1, 0)])
    first = jnp.where(core == 0, mine, other)
    second = jnp.where(core == 0, other, mine)
    both = jnp.stack([first, second], 1)
    return jnp.transpose(both, (2, 0, 1, 3, 4)).reshape(x.shape[0], n * CORES, x.shape[2], x.shape[3])


def scatter_rows(y):
    frames, rows, columns, part_width = y.shape
    me = lax.axis_index("z") * CORES + lax.axis_index("core")
    pieces = []
    for shift in range(rows):
        piece = lax.dynamic_index_in_dim(y, (me + shift) % rows, 1, keepdims=False)
        if shift:
            piece = lax.ppermute(piece, ROW_AXES, [(i, (i + shift) % rows) for i in range(rows)])
        pieces.append(piece)
    stacked = jnp.stack(pieces[::-1], 0)
    ordered = rotated(stacked, (rows - 1 - me) % rows)
    return jnp.transpose(ordered, (1, 2, 0, 3)).reshape(frames, 1, columns, rows * part_width)


def causal_conv(extended, kernel, bias_part):
    out = lax.conv_general_dilated(
        extended[None],
        kernel,
        window_strides=(1, 1, 1),
        padding=((0, 0), (1, 1), (1, 1)),
        dimension_numbers=("NDHWC", "ODHWI", "NDHWC"),
        preferred_element_type=jnp.float32,
    )
    return out[0] + bias_part


def shards(features, gain_one, weight_one, bias_one, gain_two, weight_two, bias_two):
    part_width = weight_one.shape[0]
    index = lax.axis_index("z") * CORES + lax.axis_index("core")
    offset = index * part_width
    bias_first = lax.dynamic_slice_in_dim(bias_one, offset, part_width, 0)
    bias_second = lax.dynamic_slice_in_dim(bias_two, offset, part_width, 0)
    normed_one = norm_silu(features, gain_one)
    prior_one = passed_along(normed_one, "tm", 1)
    extended_one = jnp.concatenate([prior_one, normed_one], 0)
    full_one = gather_rows(extended_one)
    conv_one = causal_conv(full_one, weight_one, bias_first).astype(jnp.bfloat16)
    own_rows = scatter_rows(conv_one)
    normed_two = norm_silu(own_rows, gain_two)
    prior_two = passed_along(normed_two, "tm", 1)
    extended_two = jnp.concatenate([prior_two, normed_two], 0)
    full_two = gather_rows(extended_two)
    conv_two = causal_conv(full_two, weight_two, bias_second)
    returned = scatter_rows(conv_two)
    return (features.astype(jnp.float32) + returned).astype(jnp.bfloat16)


def solution(mesh):
    tm = mesh.shape["tm"]
    rows = mesh.shape["rows"]
    split = Mesh(mesh.devices.reshape(tm, rows // CORES, CORES), ("tm",) + ROW_AXES)
    in_specs = (
        P("tm", ROW_AXES, None, None),
        P(),
        P(ROW_AXES, None, None, None, None),
        P(),
        P(),
        P(ROW_AXES, None, None, None, None),
        P(),
    )
    out_specs = P("tm", ROW_AXES, None, None)
    return jax.shard_map(shards, mesh=split, in_specs=in_specs, out_specs=out_specs, check_vma=False)
```

```python
import jax
import jax.numpy as jnp
from jax import lax
from jax.sharding import PartitionSpec as P


def passed_along(x, axis, by):
    peers = lax.axis_size(axis)
    pairs = [(i, i + by) for i in range(peers) if 0 <= i + by < peers]
    return lax.ppermute(x, axis, pairs)


def norm_silu(values, norm_gain):
    values = values.astype(jnp.float32)
    mean_square = jnp.mean(values * values, axis=-1, keepdims=True)
    scaled = values * lax.rsqrt(mean_square + 1e-06) * norm_gain
    return jax.nn.silu(scaled).astype(jnp.bfloat16)


def causal_conv(own, kernel, bias_part):
    part_width = kernel.shape[0]
    stacked = jnp.transpose(kernel, (1, 0, 2, 3, 4)).reshape(3 * part_width, 3, 3, kernel.shape[4])
    product = lax.conv_general_dilated(
        own,
        stacked,
        window_strides=(1, 1),
        padding=((1, 1), (1, 1)),
        dimension_numbers=("NHWC", "OHWI", "NHWC"),
        preferred_element_type=jnp.float32,
    )
    tap = [product[..., a * part_width : (a + 1) * part_width] for a in range(3)]
    onward = jnp.stack([tap[0][0] + tap[1][1], tap[0][1]], 0)
    kept = jnp.stack([tap[2][0], tap[1][0] + tap[2][1]], 0)
    arrived = passed_along(onward, "tm", 1)
    return kept + arrived + bias_part


def shards(features, gain_one, weight_one, bias_one, gain_two, weight_two, bias_two):
    part_width = weight_one.shape[0]
    offset = lax.axis_index("rows") * part_width
    bias_first = lax.dynamic_slice_in_dim(bias_one, offset, part_width, 0)
    bias_second = lax.dynamic_slice_in_dim(bias_two, offset, part_width, 0)
    normed_one = norm_silu(features, gain_one)
    full_one = lax.all_gather(normed_one, "rows", axis=1, tiled=True)
    conv_one = causal_conv(full_one, weight_one, bias_first).astype(jnp.bfloat16)
    own_rows = lax.all_to_all(conv_one, "rows", split_axis=1, concat_axis=3, tiled=True)
    normed_two = norm_silu(own_rows, gain_two)
    full_two = lax.all_gather(normed_two, "rows", axis=1, tiled=True)
    conv_two = causal_conv(full_two, weight_two, bias_second)
    returned = lax.all_to_all(conv_two, "rows", split_axis=1, concat_axis=3, tiled=True)
    return (features.astype(jnp.float32) + returned).astype(jnp.bfloat16)


def solution(mesh):
    in_specs = (
        P("tm", "rows", None, None),
        P(),
        P("rows", None, None, None, None),
        P(),
        P(),
        P("rows", None, None, None, None),
        P(),
    )
    out_specs = P("tm", "rows", None, None)
    return jax.shard_map(shards, mesh=mesh, in_specs=in_specs, out_specs=out_specs, check_vma=False)
```

```python
import jax
import jax.numpy as jnp
from jax import lax
from jax.sharding import PartitionSpec as P


def passed_along(x, axis, by):
    peers = lax.axis_size(axis)
    pairs = [(i, i + by) for i in range(peers) if 0 <= i + by < peers]
    return lax.ppermute(x, axis, pairs)


def norm_silu(values, norm_gain):
    values = values.astype(jnp.float32)
    mean_square = jnp.mean(values * values, axis=-1, keepdims=True)
    scaled = values * lax.rsqrt(mean_square + 1e-06) * norm_gain
    return jax.nn.silu(scaled).astype(jnp.bfloat16)


def causal_conv(own, kernel, bias_part):
    part_width = kernel.shape[0]
    stacked = jnp.transpose(kernel, (1, 0, 2, 3, 4)).reshape(3 * part_width, 3, 3, kernel.shape[4])
    product = lax.conv_general_dilated(
        own,
        stacked,
        window_strides=(1, 1),
        padding=((1, 1), (1, 1)),
        dimension_numbers=("NHWC", "OHWI", "NHWC"),
        preferred_element_type=jnp.float32,
    )
    tap = [product[..., a * part_width : (a + 1) * part_width] for a in range(3)]
    onward = jnp.stack([tap[0][0] + tap[1][1], tap[0][1]], 0)
    kept = jnp.stack([tap[2][0], tap[1][0] + tap[2][1]], 0)
    arrived = passed_along(onward, "tm", 1)
    return kept + arrived + bias_part


def shards(features, gain_one, weight_one, bias_one, gain_two, weight_two, bias_two):
    part_width = weight_one.shape[0]
    offset = lax.axis_index("rows") * part_width
    bias_first = lax.dynamic_slice_in_dim(bias_one, offset, part_width, 0)
    bias_second = lax.dynamic_slice_in_dim(bias_two, offset, part_width, 0)
    normed_one = norm_silu(features, gain_one)
    full_one = lax.all_gather(normed_one, "rows", axis=1, tiled=True)
    conv_one = causal_conv(full_one, weight_one, bias_first).astype(jnp.bfloat16)
    every_channel = lax.all_gather(conv_one, "rows", axis=3, tiled=True)
    full_two = norm_silu(every_channel, gain_two)
    conv_two = causal_conv(full_two, weight_two, bias_second)
    returned = lax.all_to_all(conv_two, "rows", split_axis=1, concat_axis=3, tiled=True)
    return (features.astype(jnp.float32) + returned).astype(jnp.bfloat16)


def solution(mesh):
    in_specs = (
        P("tm", "rows", None, None),
        P(),
        P("rows", None, None, None, None),
        P(),
        P(),
        P("rows", None, None, None, None),
        P(),
    )
    out_specs = P("tm", "rows", None, None)
    return jax.shard_map(shards, mesh=mesh, in_specs=in_specs, out_specs=out_specs, check_vma=False)
```

```python
import jax
import jax.numpy as jnp
from jax import lax
from jax.sharding import PartitionSpec as P


def passed_along(x, axis, by):
    peers = lax.axis_size(axis)
    pairs = [(i, i + by) for i in range(peers) if 0 <= i + by < peers]
    return lax.ppermute(x, axis, pairs)


def norm_silu(values, norm_gain):
    values = values.astype(jnp.float32)
    mean_square = jnp.mean(values * values, axis=-1, keepdims=True)
    scaled = values * lax.rsqrt(mean_square + 1e-06) * norm_gain
    return jax.nn.silu(scaled).astype(jnp.bfloat16)


def causal_conv(own, kernel, bias_part):
    part_width = kernel.shape[0]
    stacked = jnp.transpose(kernel, (1, 0, 2, 3, 4)).reshape(3 * part_width, 3, 3, kernel.shape[4])
    product = lax.conv_general_dilated(
        own,
        stacked,
        window_strides=(1, 1),
        padding=((1, 1), (1, 1)),
        dimension_numbers=("NHWC", "OHWI", "NHWC"),
        preferred_element_type=jnp.float32,
    )
    tap = [product[..., a * part_width : (a + 1) * part_width] for a in range(3)]
    onward = jnp.stack([tap[0][0] + tap[1][1], tap[0][1]], 0)
    kept = jnp.stack([tap[2][0], tap[1][0] + tap[2][1]], 0)
    arrived = passed_along(onward.reshape(onward.shape[0], -1), "tm", 1).reshape(onward.shape)
    return kept + arrived + bias_part


def shards(features, gain_one, weight_one, bias_one, gain_two, weight_two, bias_two):
    part_width = weight_one.shape[0]
    offset = lax.axis_index("rows") * part_width
    bias_first = lax.dynamic_slice_in_dim(bias_one, offset, part_width, 0)
    bias_second = lax.dynamic_slice_in_dim(bias_two, offset, part_width, 0)
    normed_one = norm_silu(features, gain_one)
    full_one = lax.all_gather(normed_one, "rows", axis=1, tiled=True)
    conv_one = causal_conv(full_one, weight_one, bias_first).astype(jnp.bfloat16)
    frames, height, columns, _ = conv_one.shape
    blocks = lax.all_gather(conv_one.reshape(frames, -1), "rows", axis=0, tiled=False)
    blocks = blocks.reshape(-1, frames, height, columns, part_width)
    every_channel = jnp.transpose(blocks, (1, 2, 3, 0, 4)).reshape(frames, height, columns, -1)
    full_two = norm_silu(every_channel, gain_two)
    conv_two = causal_conv(full_two, weight_two, bias_second)
    returned = lax.all_to_all(conv_two, "rows", split_axis=1, concat_axis=3, tiled=True)
    return (features.astype(jnp.float32) + returned).astype(jnp.bfloat16)


def solution(mesh):
    in_specs = (
        P("tm", "rows", None, None),
        P(),
        P("rows", None, None, None, None),
        P(),
        P(),
        P("rows", None, None, None, None),
        P(),
    )
    out_specs = P("tm", "rows", None, None)
    return jax.shard_map(shards, mesh=mesh, in_specs=in_specs, out_specs=out_specs, check_vma=False)
```

```python
import jax
import jax.numpy as jnp
from jax import lax
from jax.sharding import PartitionSpec as P


def passed_along(x, axis, by):
    peers = lax.axis_size(axis)
    pairs = [(i, i + by) for i in range(peers) if 0 <= i + by < peers]
    return lax.ppermute(x, axis, pairs)


def norm_silu(values, norm_gain):
    values = values.astype(jnp.float32)
    mean_square = jnp.mean(values * values, axis=-1, keepdims=True)
    scaled = values * lax.rsqrt(mean_square + 1e-06) * norm_gain
    return jax.nn.silu(scaled).astype(jnp.bfloat16)


def causal_conv(own, kernel, bias_part):
    part_width = kernel.shape[0]
    stacked = jnp.transpose(kernel, (1, 0, 2, 3, 4)).reshape(3 * part_width, 3, 3, kernel.shape[4])
    product = lax.conv_general_dilated(
        own,
        stacked,
        window_strides=(1, 1),
        padding=((1, 1), (1, 1)),
        dimension_numbers=("NHWC", "OHWI", "NHWC"),
        preferred_element_type=jnp.float32,
    )
    tap = [product[..., a * part_width : (a + 1) * part_width] for a in range(3)]
    onward = jnp.stack([tap[0][0] + tap[1][1], tap[0][1]], 0)
    kept = jnp.stack([tap[2][0], tap[1][0] + tap[2][1]], 0)
    arrived = passed_along(onward.reshape(onward.shape[0], -1), "tm", 1).reshape(onward.shape)
    return kept + arrived + bias_part


def shards(features, gain_one, weight_one, bias_one, gain_two, weight_two, bias_two):
    part_width = weight_one.shape[0]
    offset = lax.axis_index("rows") * part_width
    bias_first = lax.dynamic_slice_in_dim(bias_one, offset, part_width, 0)
    bias_second = lax.dynamic_slice_in_dim(bias_two, offset, part_width, 0)
    normed_one = norm_silu(features, gain_one)
    full_one = lax.all_gather(normed_one, "rows", axis=1, tiled=True)
    conv_one = causal_conv(full_one, weight_one, bias_first).astype(jnp.bfloat16)
    own_rows = lax.all_to_all(conv_one, "rows", split_axis=1, concat_axis=3, tiled=True)
    normed_two = norm_silu(own_rows, gain_two)
    full_two = lax.all_gather(normed_two, "rows", axis=1, tiled=True)
    conv_two = causal_conv(full_two, weight_two, bias_second)
    returned = lax.all_to_all(conv_two, "rows", split_axis=1, concat_axis=3, tiled=True)
    return (features.astype(jnp.float32) + returned).astype(jnp.bfloat16)


def solution(mesh):
    in_specs = (
        P("tm", "rows", None, None),
        P(),
        P("rows", None, None, None, None),
        P(),
        P(),
        P("rows", None, None, None, None),
        P(),
    )
    out_specs = P("tm", "rows", None, None)
    return jax.shard_map(shards, mesh=mesh, in_specs=in_specs, out_specs=out_specs, check_vma=False)
```

```python
import jax
import jax.numpy as jnp
from jax import lax
from jax.sharding import PartitionSpec as P


def passed_along(x, axis, by):
    peers = lax.axis_size(axis)
    pairs = [(i, i + by) for i in range(peers) if 0 <= i + by < peers]
    return lax.ppermute(x, axis, pairs)


def norm_silu(values, norm_gain):
    values = values.astype(jnp.float32)
    mean_square = jnp.mean(values * values, axis=-1, keepdims=True)
    scaled = values * lax.rsqrt(mean_square + 1e-06) * norm_gain
    return jax.nn.silu(scaled).astype(jnp.bfloat16)


def causal_conv(own, kernel, bias_part):
    part_width = kernel.shape[0]
    stacked = jnp.transpose(kernel, (1, 0, 2, 3, 4)).reshape(3 * part_width, 3, 3, kernel.shape[4])
    product = lax.conv_general_dilated(
        own,
        stacked,
        window_strides=(1, 1),
        padding=((1, 1), (1, 1)),
        dimension_numbers=("NHWC", "OHWI", "NHWC"),
        preferred_element_type=jnp.float32,
    )
    tap = [product[..., a * part_width : (a + 1) * part_width] for a in range(3)]
    onward = jnp.stack([tap[0][0] + tap[1][1], tap[0][1]], 0)
    kept = jnp.stack([tap[2][0], tap[1][0] + tap[2][1]], 0)
    sent = onward.reshape(onward.shape[0], -1).astype(jnp.bfloat16)
    arrived = passed_along(sent, "tm", 1).reshape(onward.shape).astype(jnp.float32)
    return kept + arrived + bias_part


def shards(features, gain_one, weight_one, bias_one, gain_two, weight_two, bias_two):
    part_width = weight_one.shape[0]
    offset = lax.axis_index("rows") * part_width
    bias_first = lax.dynamic_slice_in_dim(bias_one, offset, part_width, 0)
    bias_second = lax.dynamic_slice_in_dim(bias_two, offset, part_width, 0)
    normed_one = norm_silu(features, gain_one)
    full_one = lax.all_gather(normed_one, "rows", axis=1, tiled=True)
    conv_one = causal_conv(full_one, weight_one, bias_first).astype(jnp.bfloat16)
    own_rows = lax.all_to_all(conv_one, "rows", split_axis=1, concat_axis=3, tiled=True)
    normed_two = norm_silu(own_rows, gain_two)
    full_two = lax.all_gather(normed_two, "rows", axis=1, tiled=True)
    conv_two = causal_conv(full_two, weight_two, bias_second)
    returned = lax.all_to_all(conv_two, "rows", split_axis=1, concat_axis=3, tiled=True)
    return (features.astype(jnp.float32) + returned).astype(jnp.bfloat16)


def solution(mesh):
    in_specs = (
        P("tm", "rows", None, None),
        P(),
        P("rows", None, None, None, None),
        P(),
        P(),
        P("rows", None, None, None, None),
        P(),
    )
    out_specs = P("tm", "rows", None, None)
    return jax.shard_map(shards, mesh=mesh, in_specs=in_specs, out_specs=out_specs, check_vma=False)
```

```python
import jax
import jax.numpy as jnp
from jax import lax
from jax.sharding import PartitionSpec as P


def passed_along(x, axis, by):
    peers = lax.axis_size(axis)
    pairs = [(i, i + by) for i in range(peers) if 0 <= i + by < peers]
    return lax.ppermute(x, axis, pairs)


def norm_silu(values, norm_gain):
    values = values.astype(jnp.float32)
    mean_square = jnp.mean(values * values, axis=-1, keepdims=True)
    scaled = values * lax.rsqrt(mean_square + 1e-06) * norm_gain
    return jax.nn.silu(scaled).astype(jnp.bfloat16)


def causal_conv(own, kernel, bias_part):
    part_width = kernel.shape[0]
    stacked = jnp.transpose(kernel, (1, 0, 2, 3, 4)).reshape(3 * part_width, 3, 3, kernel.shape[4])
    product = lax.conv_general_dilated(
        own,
        stacked,
        window_strides=(1, 1),
        padding=((1, 1), (1, 1)),
        dimension_numbers=("NHWC", "OHWI", "NHWC"),
        preferred_element_type=jnp.float32,
    )
    tap = [product[..., a * part_width : (a + 1) * part_width] for a in range(3)]
    onward = jnp.stack([tap[0][0] + tap[1][1], tap[0][1]], 0)
    kept = jnp.stack([tap[2][0], tap[1][0] + tap[2][1]], 0)
    arrived = passed_along(onward.reshape(onward.shape[0], -1), "tm", 1).reshape(onward.shape)
    return kept + arrived + bias_part


def shards(features, gain_one, weight_one, bias_one, gain_two, weight_two, bias_two):
    part_width = weight_one.shape[0]
    offset = lax.axis_index("rows") * part_width
    bias_first = lax.dynamic_slice_in_dim(bias_one, offset, part_width, 0)
    bias_second = lax.dynamic_slice_in_dim(bias_two, offset, part_width, 0)
    normed_one = norm_silu(features, gain_one)
    full_one = lax.all_gather(normed_one, "rows", axis=1, tiled=True)
    conv_one = causal_conv(full_one, weight_one, bias_first).astype(jnp.bfloat16)
    own_rows = lax.all_to_all(conv_one, "rows", split_axis=1, concat_axis=3, tiled=True)
    normed_two = norm_silu(own_rows, gain_two)
    full_two = lax.all_gather(normed_two, "rows", axis=1, tiled=True)
    conv_two = causal_conv(full_two, weight_two, bias_second)
    high = conv_two.astype(jnp.bfloat16)
    low = (conv_two - high.astype(jnp.float32)).astype(jnp.bfloat16)
    pair = jnp.concatenate([high, low], 0)
    returned = lax.all_to_all(pair, "rows", split_axis=1, concat_axis=3, tiled=True).astype(jnp.float32)
    frames = conv_two.shape[0]
    total = returned[:frames] + returned[frames:]
    return (features.astype(jnp.float32) + total).astype(jnp.bfloat16)


def solution(mesh):
    in_specs = (
        P("tm", "rows", None, None),
        P(),
        P("rows", None, None, None, None),
        P(),
        P(),
        P("rows", None, None, None, None),
        P(),
    )
    out_specs = P("tm", "rows", None, None)
    return jax.shard_map(shards, mesh=mesh, in_specs=in_specs, out_specs=out_specs, check_vma=False)
```

```python
import jax
import jax.numpy as jnp
from jax import lax
from jax.sharding import PartitionSpec as P


def passed_along(x, axis, by):
    peers = lax.axis_size(axis)
    pairs = [(i, i + by) for i in range(peers) if 0 <= i + by < peers]
    return lax.ppermute(x, axis, pairs)


def norm_silu(values, norm_gain):
    values = values.astype(jnp.float32)
    mean_square = jnp.mean(values * values, axis=-1, keepdims=True)
    scaled = values * lax.rsqrt(mean_square + 1e-06) * norm_gain
    return jax.nn.silu(scaled).astype(jnp.bfloat16)


def causal_conv(own, kernel, bias_part):
    part_width = kernel.shape[0]
    frames, height, columns, _ = own.shape
    stacked = jnp.transpose(kernel, (1, 0, 2, 3, 4)).reshape(3 * part_width, 3, 3, kernel.shape[4])
    product = lax.conv_general_dilated(
        own,
        stacked,
        window_strides=(1, 1),
        padding=((1, 1), (1, 1)),
        dimension_numbers=("NHWC", "OHWI", "NHWC"),
        preferred_element_type=jnp.float32,
    )
    tap = [product[..., a * part_width : (a + 1) * part_width] for a in range(3)]

    def rows_first(pair):
        return jnp.transpose(jnp.stack(pair, 0), (1, 0, 2, 3)).reshape(height, -1)

    onward = rows_first([tap[0][0] + tap[1][1], tap[0][1]])
    kept = rows_first([tap[2][0], tap[1][0] + tap[2][1]])
    arrived = passed_along(onward, "tm", 1)
    return kept + arrived + jnp.tile(bias_part, frames * columns)


def own_row(laid, frames, columns):
    sources = lax.all_to_all(laid, "rows", split_axis=0, concat_axis=0, tiled=True)
    sources = sources.reshape(sources.shape[0], frames, columns, -1)
    return jnp.transpose(sources, (1, 2, 0, 3)).reshape(frames, 1, columns, -1)


def shards(features, gain_one, weight_one, bias_one, gain_two, weight_two, bias_two):
    part_width = weight_one.shape[0]
    frames, _, columns, _ = features.shape
    offset = lax.axis_index("rows") * part_width
    bias_first = lax.dynamic_slice_in_dim(bias_one, offset, part_width, 0)
    bias_second = lax.dynamic_slice_in_dim(bias_two, offset, part_width, 0)
    normed_one = norm_silu(features, gain_one)
    full_one = lax.all_gather(normed_one, "rows", axis=1, tiled=True)
    conv_one = causal_conv(full_one, weight_one, bias_first).astype(jnp.bfloat16)
    own_rows = own_row(conv_one, frames, columns)
    normed_two = norm_silu(own_rows, gain_two)
    full_two = lax.all_gather(normed_two, "rows", axis=1, tiled=True)
    conv_two = causal_conv(full_two, weight_two, bias_second)
    returned = own_row(conv_two, frames, columns)
    return (features.astype(jnp.float32) + returned).astype(jnp.bfloat16)


def solution(mesh):
    in_specs = (
        P("tm", "rows", None, None),
        P(),
        P("rows", None, None, None, None),
        P(),
        P(),
        P("rows", None, None, None, None),
        P(),
    )
    out_specs = P("tm", "rows", None, None)
    return jax.shard_map(shards, mesh=mesh, in_specs=in_specs, out_specs=out_specs, check_vma=False)
```

```python
import jax
import jax.numpy as jnp
from jax import lax
from jax.sharding import PartitionSpec as P


def passed_along(x, axis, by):
    peers = lax.axis_size(axis)
    pairs = [(i, i + by) for i in range(peers) if 0 <= i + by < peers]
    return lax.ppermute(x, axis, pairs)


def norm_silu(values, norm_gain):
    values = values.astype(jnp.float32)
    mean_square = jnp.mean(values * values, axis=-1, keepdims=True)
    scaled = values * lax.rsqrt(mean_square + 1e-06) * norm_gain
    return jax.nn.silu(scaled).astype(jnp.bfloat16)


def causal_conv(own, kernel, bias_part):
    part_width = kernel.shape[0]
    frames, height, columns, _ = own.shape
    stacked = jnp.transpose(kernel, (1, 2, 0, 3, 4)).reshape(9 * part_width, 1, 3, kernel.shape[4])
    product = lax.conv_general_dilated(
        own,
        stacked,
        window_strides=(1, 1),
        padding=((0, 0), (1, 1)),
        dimension_numbers=("NHWC", "OHWI", "NHWC"),
        preferred_element_type=jnp.float32,
    )
    padded = jnp.pad(product, ((0, 0), (1, 1), (0, 0), (0, 0)))
    tap = []
    for a in range(3):
        summed = 0
        for b in range(3):
            at = (a * 3 + b) * part_width
            summed = summed + padded[:, b : b + height, :, at : at + part_width]
        tap.append(summed)

    def rows_first(pair):
        return jnp.transpose(jnp.stack(pair, 0), (1, 0, 2, 3)).reshape(height, -1)

    onward = rows_first([tap[0][0] + tap[1][1], tap[0][1]])
    kept = rows_first([tap[2][0], tap[1][0] + tap[2][1]])
    arrived = passed_along(onward, "tm", 1)
    return kept + arrived + jnp.tile(bias_part, frames * columns)


def own_row(laid, frames, columns):
    sources = lax.all_to_all(laid, "rows", split_axis=0, concat_axis=0, tiled=True)
    sources = sources.reshape(sources.shape[0], frames, columns, -1)
    return jnp.transpose(sources, (1, 2, 0, 3)).reshape(frames, 1, columns, -1)


def shards(features, gain_one, weight_one, bias_one, gain_two, weight_two, bias_two):
    part_width = weight_one.shape[0]
    frames, _, columns, _ = features.shape
    offset = lax.axis_index("rows") * part_width
    bias_first = lax.dynamic_slice_in_dim(bias_one, offset, part_width, 0)
    bias_second = lax.dynamic_slice_in_dim(bias_two, offset, part_width, 0)
    normed_one = norm_silu(features, gain_one)
    full_one = lax.all_gather(normed_one, "rows", axis=1, tiled=True)
    conv_one = causal_conv(full_one, weight_one, bias_first).astype(jnp.bfloat16)
    own_rows = own_row(conv_one, frames, columns)
    normed_two = norm_silu(own_rows, gain_two)
    full_two = lax.all_gather(normed_two, "rows", axis=1, tiled=True)
    conv_two = causal_conv(full_two, weight_two, bias_second)
    returned = own_row(conv_two, frames, columns)
    return (features.astype(jnp.float32) + returned).astype(jnp.bfloat16)


def solution(mesh):
    in_specs = (
        P("tm", "rows", None, None),
        P(),
        P("rows", None, None, None, None),
        P(),
        P(),
        P("rows", None, None, None, None),
        P(),
    )
    out_specs = P("tm", "rows", None, None)
    return jax.shard_map(shards, mesh=mesh, in_specs=in_specs, out_specs=out_specs, check_vma=False)
```

```python
import jax
import jax.numpy as jnp
from jax import lax
from jax.sharding import PartitionSpec as P


def passed_along(x, axis, by):
    peers = lax.axis_size(axis)
    pairs = [(i, i + by) for i in range(peers) if 0 <= i + by < peers]
    return lax.ppermute(x, axis, pairs)


def norm_silu(values, norm_gain):
    values = values.astype(jnp.float32)
    mean_square = jnp.mean(values * values, axis=-1, keepdims=True)
    scaled = values * lax.rsqrt(mean_square + 1e-06) * norm_gain
    return jax.nn.silu(scaled).astype(jnp.bfloat16)


def causal_conv(own, kernel, bias_part):
    part_width = kernel.shape[0]
    frames, height, columns, _ = own.shape
    stacked = jnp.transpose(kernel, (1, 0, 2, 3, 4)).reshape(3 * part_width, 3, 3, kernel.shape[4])
    product = lax.conv_general_dilated(
        own,
        stacked,
        window_strides=(1, 1),
        padding=((1, 1), (1, 1)),
        dimension_numbers=("NHWC", "OHWI", "NHWC"),
        preferred_element_type=jnp.float32,
    )
    tap = [product[..., a * part_width : (a + 1) * part_width] for a in range(3)]

    def rows_first(pair):
        return jnp.transpose(jnp.stack(pair, 0), (1, 0, 2, 3)).reshape(height, -1)

    onward = rows_first([tap[0][0] + tap[1][1], tap[0][1]])
    kept = rows_first([tap[2][0], tap[1][0] + tap[2][1]])
    arrived = passed_along(onward, "tm", 1)
    return kept + arrived + jnp.tile(bias_part, frames * columns)


def own_row(laid, frames, columns):
    sources = lax.all_to_all(laid, "rows", split_axis=0, concat_axis=0, tiled=True)
    sources = sources.reshape(sources.shape[0], frames, columns, -1)
    return jnp.transpose(sources, (1, 2, 0, 3)).reshape(frames, 1, columns, -1)


def shards(features, gain_one, weight_one, bias_one, gain_two, weight_two, bias_two):
    part_width = weight_one.shape[0]
    frames, _, columns, _ = features.shape
    offset = lax.axis_index("rows") * part_width
    bias_first = lax.dynamic_slice_in_dim(bias_one, offset, part_width, 0)
    bias_second = lax.dynamic_slice_in_dim(bias_two, offset, part_width, 0)
    full_one = norm_silu(lax.all_gather(features, "rows", axis=1, tiled=True), gain_one)
    conv_one = causal_conv(full_one, weight_one, bias_first).astype(jnp.bfloat16)
    own_rows = own_row(conv_one, frames, columns)
    normed_two = norm_silu(own_rows, gain_two)
    full_two = lax.all_gather(normed_two, "rows", axis=1, tiled=True)
    conv_two = causal_conv(full_two, weight_two, bias_second)
    returned = own_row(conv_two, frames, columns)
    return (features.astype(jnp.float32) + returned).astype(jnp.bfloat16)


def solution(mesh):
    in_specs = (
        P("tm", "rows", None, None),
        P(),
        P("rows", None, None, None, None),
        P(),
        P(),
        P("rows", None, None, None, None),
        P(),
    )
    out_specs = P("tm", "rows", None, None)
    return jax.shard_map(shards, mesh=mesh, in_specs=in_specs, out_specs=out_specs, check_vma=False)
```

```python
import jax
import jax.numpy as jnp
from jax import lax
from jax.sharding import PartitionSpec as P


def passed_along(x, axis, by):
    peers = lax.axis_size(axis)
    pairs = [(i, i + by) for i in range(peers) if 0 <= i + by < peers]
    return lax.ppermute(x, axis, pairs)


def norm_silu(values, norm_gain):
    values = values.astype(jnp.float32)
    mean_square = jnp.mean(values * values, axis=-1, keepdims=True)
    scaled = values * lax.rsqrt(mean_square + 1e-06) * norm_gain
    return jax.nn.silu(scaled).astype(jnp.bfloat16)


def causal_conv(own, kernel, bias_part):
    part_width = kernel.shape[0]
    frames, height, columns, _ = own.shape
    stacked = jnp.transpose(kernel, (1, 0, 2, 3, 4)).reshape(3 * part_width, 3, 3, kernel.shape[4])
    product = lax.conv_general_dilated(
        own,
        stacked,
        window_strides=(1, 1),
        padding=((1, 1), (1, 1)),
        dimension_numbers=("NHWC", "OHWI", "NHWC"),
        preferred_element_type=jnp.float32,
    )
    tap = [product[..., a * part_width : (a + 1) * part_width] for a in range(3)]

    def rows_first(pair):
        return jnp.transpose(jnp.stack(pair, 0), (1, 0, 2, 3)).reshape(height, -1)

    onward = rows_first([tap[0][0] + tap[1][1], tap[0][1]])
    kept = rows_first([tap[2][0], tap[1][0] + tap[2][1]])
    arrived = passed_along(onward, "tm", 1)
    return kept + arrived + jnp.tile(bias_part, frames * columns)


def own_row(laid, frames, columns):
    sources = lax.all_to_all(laid, "rows", split_axis=0, concat_axis=0, tiled=True)
    sources = sources.reshape(sources.shape[0], frames, columns, -1)
    return jnp.transpose(sources, (1, 2, 0, 3)).reshape(frames, 1, columns, -1)


def shards(features, gain_one, weight_one, bias_one, gain_two, weight_two, bias_two):
    part_width = weight_one.shape[0]
    frames, _, columns, _ = features.shape
    offset = lax.axis_index("rows") * part_width
    bias_first = lax.dynamic_slice_in_dim(bias_one, offset, part_width, 0)
    bias_second = lax.dynamic_slice_in_dim(bias_two, offset, part_width, 0)
    every_row = lax.all_gather(features, "rows", axis=1, tiled=True)
    full_one = norm_silu(every_row, gain_one)
    residual = lax.dynamic_slice_in_dim(every_row, offset, part_width, 3)
    residual = jnp.transpose(residual, (1, 0, 2, 3)).reshape(residual.shape[1], -1)
    conv_one = causal_conv(full_one, weight_one, bias_first).astype(jnp.bfloat16)
    own_rows = own_row(conv_one, frames, columns)
    normed_two = norm_silu(own_rows, gain_two)
    full_two = lax.all_gather(normed_two, "rows", axis=1, tiled=True)
    conv_two = causal_conv(full_two, weight_two, bias_second)
    block_out = (residual.astype(jnp.float32) + conv_two).astype(jnp.bfloat16)
    return own_row(block_out, frames, columns)


def solution(mesh):
    in_specs = (
        P("tm", "rows", None, None),
        P(),
        P("rows", None, None, None, None),
        P(),
        P(),
        P("rows", None, None, None, None),
        P(),
    )
    out_specs = P("tm", "rows", None, None)
    return jax.shard_map(shards, mesh=mesh, in_specs=in_specs, out_specs=out_specs, check_vma=False)
```

```python
import jax
import jax.numpy as jnp
from jax import lax
from jax.sharding import PartitionSpec as P


def passed_along(x, axis, by):
    peers = lax.axis_size(axis)
    pairs = [(i, i + by) for i in range(peers) if 0 <= i + by < peers]
    return lax.ppermute(x, axis, pairs)


def norm_silu(values, norm_gain):
    values = values.astype(jnp.float32)
    mean_square = jnp.mean(values * values, axis=-1, keepdims=True)
    scaled = values * lax.rsqrt(mean_square + 1e-06) * norm_gain
    return jax.nn.silu(scaled).astype(jnp.bfloat16)


def causal_conv(own, kernel, bias_part):
    part_width = kernel.shape[0]
    frames, height, columns, _ = own.shape
    stacked = jnp.transpose(kernel, (1, 0, 2, 3, 4)).reshape(3 * part_width, 3, 3, kernel.shape[4])
    product = lax.conv_general_dilated(
        own,
        stacked,
        window_strides=(1, 1),
        padding=((1, 1), (1, 1)),
        dimension_numbers=("NHWC", "OHWI", "NHWC"),
        preferred_element_type=jnp.float32,
    )
    tap = [product[..., a * part_width : (a + 1) * part_width] for a in range(3)]

    def rows_first(pair):
        return jnp.transpose(jnp.stack(pair, 0), (1, 0, 2, 3)).reshape(height, frames, -1)

    onward = rows_first([tap[0][0] + tap[1][1], tap[0][1]])
    kept = rows_first([tap[2][0], tap[1][0] + tap[2][1]])
    arrived = passed_along(onward.reshape(height, -1), "tm", 1).reshape(kept.shape)
    return kept + arrived + jnp.tile(bias_part, columns)


def own_row(laid, frames, columns):
    sources = lax.all_to_all(laid, "rows", split_axis=0, concat_axis=0, tiled=True)
    sources = sources.reshape(sources.shape[0], frames, columns, -1)
    return jnp.transpose(sources, (1, 2, 0, 3)).reshape(frames, 1, columns, -1)


def shards(features, gain_one, weight_one, bias_one, gain_two, weight_two, bias_two):
    part_width = weight_one.shape[0]
    frames, _, columns, _ = features.shape
    offset = lax.axis_index("rows") * part_width
    bias_first = lax.dynamic_slice_in_dim(bias_one, offset, part_width, 0)
    bias_second = lax.dynamic_slice_in_dim(bias_two, offset, part_width, 0)
    every_row = lax.all_gather(features, "rows", axis=1, tiled=True)
    full_one = norm_silu(every_row, gain_one)
    residual = lax.dynamic_slice_in_dim(every_row, offset, part_width, 3)
    residual = jnp.transpose(residual, (1, 0, 2, 3)).reshape(residual.shape[1], frames, -1)
    conv_one = causal_conv(full_one, weight_one, bias_first).astype(jnp.bfloat16)
    own_rows = own_row(conv_one, frames, columns)
    normed_two = norm_silu(own_rows, gain_two)
    full_two = lax.all_gather(normed_two, "rows", axis=1, tiled=True)
    conv_two = causal_conv(full_two, weight_two, bias_second)
    block_out = (residual.astype(jnp.float32) + conv_two).astype(jnp.bfloat16)
    return own_row(block_out, frames, columns)


def solution(mesh):
    in_specs = (
        P("tm", "rows", None, None),
        P(),
        P("rows", None, None, None, None),
        P(),
        P(),
        P("rows", None, None, None, None),
        P(),
    )
    out_specs = P("tm", "rows", None, None)
    return jax.shard_map(shards, mesh=mesh, in_specs=in_specs, out_specs=out_specs, check_vma=False)
```

```python
import jax
import jax.numpy as jnp
from jax import lax
from jax.sharding import PartitionSpec as P


def passed_along(x, axis, by):
    peers = lax.axis_size(axis)
    pairs = [(i, i + by) for i in range(peers) if 0 <= i + by < peers]
    return lax.ppermute(x, axis, pairs)


def norm_silu(values, norm_gain):
    values = values.astype(jnp.float32)
    mean_square = jnp.mean(values * values, axis=-1, keepdims=True)
    scaled = values * lax.rsqrt(mean_square + 1e-06) * norm_gain
    return jax.nn.silu(scaled).astype(jnp.bfloat16)


def causal_conv(own, kernel, bias_part):
    part_width = kernel.shape[0]
    frames, height, columns, _ = own.shape
    stacked = jnp.transpose(kernel, (1, 0, 2, 3, 4)).reshape(3 * part_width, 3, 3, kernel.shape[4])
    product = lax.conv_general_dilated(
        own,
        stacked,
        window_strides=(1, 1),
        padding=((1, 1), (1, 1)),
        dimension_numbers=("NHWC", "OHWI", "HNWC"),
        preferred_element_type=jnp.float32,
    )
    tap = [product[..., a * part_width : (a + 1) * part_width] for a in range(3)]

    def rows_first(pair):
        return jnp.stack(pair, 1).reshape(height, frames, -1)

    onward = rows_first([tap[0][:, 0] + tap[1][:, 1], tap[0][:, 1]])
    kept = rows_first([tap[2][:, 0], tap[1][:, 0] + tap[2][:, 1]])
    arrived = passed_along(onward.reshape(height, -1), "tm", 1).reshape(kept.shape)
    return kept + arrived + jnp.tile(bias_part, columns)


def own_row(laid, frames, columns):
    sources = lax.all_to_all(laid, "rows", split_axis=0, concat_axis=0, tiled=True)
    sources = sources.reshape(sources.shape[0], frames, columns, -1)
    return jnp.transpose(sources, (1, 2, 0, 3)).reshape(frames, 1, columns, -1)


def shards(features, gain_one, weight_one, bias_one, gain_two, weight_two, bias_two):
    part_width = weight_one.shape[0]
    frames, _, columns, _ = features.shape
    offset = lax.axis_index("rows") * part_width
    bias_first = lax.dynamic_slice_in_dim(bias_one, offset, part_width, 0)
    bias_second = lax.dynamic_slice_in_dim(bias_two, offset, part_width, 0)
    every_row = lax.all_gather(features, "rows", axis=1, tiled=True)
    full_one = norm_silu(every_row, gain_one)
    residual = lax.dynamic_slice_in_dim(every_row, offset, part_width, 3)
    residual = jnp.transpose(residual, (1, 0, 2, 3)).reshape(residual.shape[1], frames, -1)
    conv_one = causal_conv(full_one, weight_one, bias_first).astype(jnp.bfloat16)
    own_rows = own_row(conv_one, frames, columns)
    normed_two = norm_silu(own_rows, gain_two)
    full_two = lax.all_gather(normed_two, "rows", axis=1, tiled=True)
    conv_two = causal_conv(full_two, weight_two, bias_second)
    block_out = (residual.astype(jnp.float32) + conv_two).astype(jnp.bfloat16)
    return own_row(block_out, frames, columns)


def solution(mesh):
    in_specs = (
        P("tm", "rows", None, None),
        P(),
        P("rows", None, None, None, None),
        P(),
        P(),
        P("rows", None, None, None, None),
        P(),
    )
    out_specs = P("tm", "rows", None, None)
    return jax.shard_map(shards, mesh=mesh, in_specs=in_specs, out_specs=out_specs, check_vma=False)
```

```python
import jax
import jax.numpy as jnp
from jax import lax
from jax.sharding import PartitionSpec as P


def passed_along(x, axis, by):
    peers = lax.axis_size(axis)
    pairs = [(i, i + by) for i in range(peers) if 0 <= i + by < peers]
    return lax.ppermute(x, axis, pairs)


def norm_silu(values, norm_gain):
    values = values.astype(jnp.float32)
    mean_square = jnp.mean(values * values, axis=-1, keepdims=True)
    scaled = values * lax.rsqrt(mean_square + 1e-06) * norm_gain
    return jax.nn.silu(scaled).astype(jnp.bfloat16)


def causal_conv(own, kernel, bias_part):
    part_width = kernel.shape[0]
    frames, height, columns, _ = own.shape
    stacked = jnp.transpose(kernel, (1, 0, 2, 3, 4)).reshape(3 * part_width, 3, 3, kernel.shape[4])
    product = lax.conv_general_dilated(
        own,
        stacked,
        window_strides=(1, 1),
        padding=((1, 1), (1, 1)),
        dimension_numbers=("NHWC", "OHWI", "NHWC"),
        preferred_element_type=jnp.float32,
    )
    tap = [product[..., a * part_width : (a + 1) * part_width] for a in range(3)]

    def rows_first(pair):
        return jnp.transpose(jnp.stack(pair, 0), (1, 0, 2, 3)).reshape(height, frames, -1)

    onward = rows_first([tap[0][0] + tap[1][1], tap[0][1]])
    kept = rows_first([tap[2][0], tap[1][0] + tap[2][1]])
    arrived = passed_along(onward.reshape(height, -1), "tm", 1).reshape(kept.shape)
    return kept + arrived + jnp.tile(bias_part, columns)


def own_row(laid, frames, columns):
    pieces = laid.reshape(laid.shape[0], frames, columns, -1)
    placed = lax.all_to_all(pieces, "rows", split_axis=0, concat_axis=3, tiled=True)
    return placed.reshape(frames, 1, columns, -1)


def shards(features, gain_one, weight_one, bias_one, gain_two, weight_two, bias_two):
    part_width = weight_one.shape[0]
    frames, _, columns, _ = features.shape
    offset = lax.axis_index("rows") * part_width
    bias_first = lax.dynamic_slice_in_dim(bias_one, offset, part_width, 0)
    bias_second = lax.dynamic_slice_in_dim(bias_two, offset, part_width, 0)
    every_row = lax.all_gather(features, "rows", axis=1, tiled=True)
    full_one = norm_silu(every_row, gain_one)
    residual = lax.dynamic_slice_in_dim(every_row, offset, part_width, 3)
    residual = jnp.transpose(residual, (1, 0, 2, 3)).reshape(residual.shape[1], frames, -1)
    conv_one = causal_conv(full_one, weight_one, bias_first).astype(jnp.bfloat16)
    own_rows = own_row(conv_one, frames, columns)
    normed_two = norm_silu(own_rows, gain_two)
    full_two = lax.all_gather(normed_two, "rows", axis=1, tiled=True)
    conv_two = causal_conv(full_two, weight_two, bias_second)
    block_out = (residual.astype(jnp.float32) + conv_two).astype(jnp.bfloat16)
    return own_row(block_out, frames, columns)


def solution(mesh):
    in_specs = (
        P("tm", "rows", None, None),
        P(),
        P("rows", None, None, None, None),
        P(),
        P(),
        P("rows", None, None, None, None),
        P(),
    )
    out_specs = P("tm", "rows", None, None)
    return jax.shard_map(shards, mesh=mesh, in_specs=in_specs, out_specs=out_specs, check_vma=False)
```

```python
import jax
import jax.numpy as jnp
from jax import lax
from jax.sharding import PartitionSpec as P


def passed_along(x, axis, by):
    peers = lax.axis_size(axis)
    pairs = [(i, i + by) for i in range(peers) if 0 <= i + by < peers]
    return lax.ppermute(x, axis, pairs)


def norm_silu(values, norm_gain):
    values = values.astype(jnp.float32)
    mean_square = jnp.mean(values * values, axis=-1, keepdims=True)
    scaled = values * lax.rsqrt(mean_square + 1e-06) * norm_gain
    return jax.nn.silu(scaled).astype(jnp.bfloat16)


def causal_conv(own, kernel, bias_part):
    part_width = kernel.shape[0]
    frames, height, columns, _ = own.shape
    stacked = jnp.transpose(kernel, (1, 0, 2, 3, 4)).reshape(3 * part_width, 3, 3, kernel.shape[4])
    product = lax.conv_general_dilated(
        own,
        stacked,
        window_strides=(1, 1),
        padding=((1, 1), (1, 1)),
        dimension_numbers=("NHWC", "OHWI", "NHWC"),
        preferred_element_type=jnp.float32,
    )
    tap = [product[..., a * part_width : (a + 1) * part_width] for a in range(3)]

    def rows_first(pair):
        return jnp.transpose(jnp.stack(pair, 0), (1, 0, 2, 3)).reshape(height, frames, -1)

    onward = rows_first([tap[0][0] + tap[1][1], tap[0][1]])
    kept = rows_first([tap[2][0], tap[1][0] + tap[2][1]])
    arrived = passed_along(onward.reshape(height, -1), "tm", 1).reshape(kept.shape)
    return kept + arrived + jnp.tile(bias_part, columns)


def own_row(laid, frames, columns):
    sources = lax.all_to_all(laid, "rows", split_axis=0, concat_axis=0, tiled=True)
    sources = sources.reshape(sources.shape[0], frames, columns, -1)
    return jnp.transpose(sources, (1, 2, 0, 3)).reshape(frames, 1, columns, -1)


def shards(features, gain_one, weight_one, bias_one, gain_two, weight_two, bias_two):
    part_width = weight_one.shape[0]
    frames, _, columns, _ = features.shape
    offset = lax.axis_index("rows") * part_width
    bias_first = lax.dynamic_slice_in_dim(bias_one, offset, part_width, 0)
    bias_second = lax.dynamic_slice_in_dim(bias_two, offset, part_width, 0)
    every_row = lax.all_gather(features, "rows", axis=1, tiled=True)
    full_one = norm_silu(every_row, gain_one)
    residual = lax.dynamic_slice_in_dim(every_row, offset, part_width, 3)
    residual = jnp.transpose(residual, (1, 0, 2, 3)).reshape(residual.shape[1], frames, -1)
    conv_one = causal_conv(full_one, weight_one, bias_first).astype(jnp.bfloat16)
    own_rows = own_row(conv_one, frames, columns)
    normed_two = norm_silu(own_rows, gain_two)
    full_two = lax.all_gather(normed_two, "rows", axis=1, tiled=True)
    conv_two = causal_conv(full_two, weight_two, bias_second)
    block_out = (residual.astype(jnp.float32) + conv_two).astype(jnp.bfloat16)
    pieces = block_out.reshape(block_out.shape[0], frames, columns, -1)
    placed = lax.all_to_all(pieces, "rows", split_axis=0, concat_axis=3, tiled=True)
    return placed.reshape(frames, 1, columns, -1)


def solution(mesh):
    in_specs = (
        P("tm", "rows", None, None),
        P(),
        P("rows", None, None, None, None),
        P(),
        P(),
        P("rows", None, None, None, None),
        P(),
    )
    out_specs = P("tm", "rows", None, None)
    return jax.shard_map(shards, mesh=mesh, in_specs=in_specs, out_specs=out_specs, check_vma=False)
```

```python
import jax
import jax.numpy as jnp
from jax import lax
from jax.sharding import PartitionSpec as P


def passed_along(x, axis, by):
    peers = lax.axis_size(axis)
    pairs = [(i, i + by) for i in range(peers) if 0 <= i + by < peers]
    return lax.ppermute(x, axis, pairs)


def norm_silu(values, norm_gain):
    values = values.astype(jnp.float32)
    mean_square = jnp.mean(values * values, axis=-1, keepdims=True)
    scaled = values * lax.rsqrt(mean_square + 1e-06) * norm_gain
    return jax.nn.silu(scaled).astype(jnp.bfloat16)


def causal_conv(own, kernel, bias_part):
    part_width = kernel.shape[0]
    frames, height, columns, _ = own.shape
    stacked = jnp.transpose(kernel, (1, 2, 0, 3, 4)).reshape(9 * part_width, 1, 3, kernel.shape[4])
    product = lax.conv_general_dilated(
        own,
        stacked,
        window_strides=(1, 1),
        padding=((0, 0), (1, 1)),
        dimension_numbers=("NHWC", "OHWI", "HNWC"),
        preferred_element_type=jnp.float32,
    )
    padded = jnp.pad(product, ((1, 1), (0, 0), (0, 0), (0, 0)))
    tap = []
    for a in range(3):
        summed = 0
        for b in range(3):
            at = (a * 3 + b) * part_width
            summed = summed + padded[b : b + height, :, :, at : at + part_width]
        tap.append(summed)

    def rows_first(pair):
        return jnp.stack(pair, 1).reshape(height, frames, -1)

    onward = rows_first([tap[0][:, 0] + tap[1][:, 1], tap[0][:, 1]])
    kept = rows_first([tap[2][:, 0], tap[1][:, 0] + tap[2][:, 1]])
    arrived = passed_along(onward.reshape(height, -1), "tm", 1).reshape(kept.shape)
    return kept + arrived + jnp.tile(bias_part, columns)


def own_row(laid, frames, columns):
    sources = lax.all_to_all(laid, "rows", split_axis=0, concat_axis=0, tiled=True)
    sources = sources.reshape(sources.shape[0], frames, columns, -1)
    return jnp.transpose(sources, (1, 2, 0, 3)).reshape(frames, 1, columns, -1)


def shards(features, gain_one, weight_one, bias_one, gain_two, weight_two, bias_two):
    part_width = weight_one.shape[0]
    frames, _, columns, _ = features.shape
    offset = lax.axis_index("rows") * part_width
    bias_first = lax.dynamic_slice_in_dim(bias_one, offset, part_width, 0)
    bias_second = lax.dynamic_slice_in_dim(bias_two, offset, part_width, 0)
    every_row = lax.all_gather(features, "rows", axis=1, tiled=True)
    full_one = norm_silu(every_row, gain_one)
    residual = lax.dynamic_slice_in_dim(every_row, offset, part_width, 3)
    residual = jnp.transpose(residual, (1, 0, 2, 3)).reshape(residual.shape[1], frames, -1)
    conv_one = causal_conv(full_one, weight_one, bias_first).astype(jnp.bfloat16)
    own_rows = own_row(conv_one, frames, columns)
    normed_two = norm_silu(own_rows, gain_two)
    full_two = lax.all_gather(normed_two, "rows", axis=1, tiled=True)
    conv_two = causal_conv(full_two, weight_two, bias_second)
    block_out = (residual.astype(jnp.float32) + conv_two).astype(jnp.bfloat16)
    return own_row(block_out, frames, columns)


def solution(mesh):
    in_specs = (
        P("tm", "rows", None, None),
        P(),
        P("rows", None, None, None, None),
        P(),
        P(),
        P("rows", None, None, None, None),
        P(),
    )
    out_specs = P("tm", "rows", None, None)
    return jax.shard_map(shards, mesh=mesh, in_specs=in_specs, out_specs=out_specs, check_vma=False)
```

```python
import jax
import jax.numpy as jnp
from jax import lax
from jax.sharding import PartitionSpec as P


def passed_along(x, axis, by):
    peers = lax.axis_size(axis)
    pairs = [(i, i + by) for i in range(peers) if 0 <= i + by < peers]
    return lax.ppermute(x, axis, pairs)


def norm_silu(values, norm_gain):
    values = values.astype(jnp.float32)
    mean_square = jnp.mean(values * values, axis=-1, keepdims=True)
    scaled = values * lax.rsqrt(mean_square + 1e-06) * norm_gain
    return jax.nn.silu(scaled).astype(jnp.bfloat16)


def stack_taps(kernel):
    return jnp.transpose(kernel, (1, 0, 2, 3, 4)).reshape(3 * kernel.shape[0], 3, 3, kernel.shape[4])


def causal_conv(own, stacked, bias_part):
    part_width = stacked.shape[0] // 3
    frames, height, columns, _ = own.shape
    product = lax.conv_general_dilated(
        own,
        stacked,
        window_strides=(1, 1),
        padding=((1, 1), (1, 1)),
        dimension_numbers=("NHWC", "OHWI", "NHWC"),
        preferred_element_type=jnp.float32,
    )
    tap = [product[..., a * part_width : (a + 1) * part_width] for a in range(3)]

    def rows_first(pair):
        return jnp.transpose(jnp.stack(pair, 0), (1, 0, 2, 3)).reshape(height, frames, -1)

    onward = rows_first([tap[0][0] + tap[1][1], tap[0][1]])
    kept = rows_first([tap[2][0], tap[1][0] + tap[2][1]])
    arrived = passed_along(onward.reshape(height, -1), "tm", 1).reshape(kept.shape)
    return kept + arrived + jnp.tile(bias_part, columns)


def own_row(laid, frames, columns):
    sources = lax.all_to_all(laid, "rows", split_axis=0, concat_axis=0, tiled=True)
    sources = sources.reshape(sources.shape[0], frames, columns, -1)
    return jnp.transpose(sources, (1, 2, 0, 3)).reshape(frames, 1, columns, -1)


def shards(features, gain_one, weight_one, bias_one, gain_two, weight_two, bias_two):
    part_width = weight_one.shape[0]
    frames, _, columns, _ = features.shape
    offset = lax.axis_index("rows") * part_width
    bias_first = lax.dynamic_slice_in_dim(bias_one, offset, part_width, 0)
    bias_second = lax.dynamic_slice_in_dim(bias_two, offset, part_width, 0)
    stacked_one = stack_taps(weight_one)
    features, stacked_one = lax.optimization_barrier((features, stacked_one))
    every_row = lax.all_gather(features, "rows", axis=1, tiled=True)
    full_one = norm_silu(every_row, gain_one)
    residual = lax.dynamic_slice_in_dim(every_row, offset, part_width, 3)
    residual = jnp.transpose(residual, (1, 0, 2, 3)).reshape(residual.shape[1], frames, -1)
    conv_one = causal_conv(full_one, stacked_one, bias_first).astype(jnp.bfloat16)
    own_rows = own_row(conv_one, frames, columns)
    normed_two = norm_silu(own_rows, gain_two)
    full_two = lax.all_gather(normed_two, "rows", axis=1, tiled=True)
    conv_two = causal_conv(full_two, stack_taps(weight_two), bias_second)
    block_out = (residual.astype(jnp.float32) + conv_two).astype(jnp.bfloat16)
    return own_row(block_out, frames, columns)


def solution(mesh):
    in_specs = (
        P("tm", "rows", None, None),
        P(),
        P("rows", None, None, None, None),
        P(),
        P(),
        P("rows", None, None, None, None),
        P(),
    )
    out_specs = P("tm", "rows", None, None)
    return jax.shard_map(shards, mesh=mesh, in_specs=in_specs, out_specs=out_specs, check_vma=False)
```

```python
import jax
import jax.numpy as jnp
from jax import lax
from jax.sharding import PartitionSpec as P


def passed_along(x, axis, by):
    peers = lax.axis_size(axis)
    pairs = [(i, i + by) for i in range(peers) if 0 <= i + by < peers]
    return lax.ppermute(x, axis, pairs)


def norm_silu(values, norm_gain):
    values = values.astype(jnp.float32)
    mean_square = jnp.mean(values * values, axis=-1, keepdims=True)
    scaled = values * lax.rsqrt(mean_square + 1e-06) * norm_gain
    return jax.nn.silu(scaled).astype(jnp.bfloat16)


def causal_conv(own, kernel, bias_part):
    part_width = kernel.shape[0]
    frames, height, columns, _ = own.shape
    stacked = jnp.transpose(kernel, (1, 0, 2, 3, 4)).reshape(3 * part_width, 3, 3, kernel.shape[4])
    product = lax.conv_general_dilated(
        own,
        stacked,
        window_strides=(1, 1),
        padding=((1, 1), (1, 1)),
        dimension_numbers=("NHWC", "OHWI", "NHWC"),
        preferred_element_type=jnp.float32,
    )
    tap = [product[..., a * part_width : (a + 1) * part_width] for a in range(3)]

    def rows_first(pair):
        return jnp.transpose(jnp.stack(pair, 0), (1, 0, 2, 3)).reshape(height, frames, -1)

    onward = rows_first([tap[0][0] + tap[1][1], tap[0][1]])
    kept = rows_first([tap[2][0], tap[1][0] + tap[2][1]]) + jnp.tile(bias_part, columns)
    kept = lax.optimization_barrier(kept)
    arrived = passed_along(onward.reshape(height, -1), "tm", 1).reshape(kept.shape)
    return kept + arrived


def own_row(laid, frames, columns):
    sources = lax.all_to_all(laid, "rows", split_axis=0, concat_axis=0, tiled=True)
    sources = sources.reshape(sources.shape[0], frames, columns, -1)
    return jnp.transpose(sources, (1, 2, 0, 3)).reshape(frames, 1, columns, -1)


def shards(features, gain_one, weight_one, bias_one, gain_two, weight_two, bias_two):
    part_width = weight_one.shape[0]
    frames, _, columns, _ = features.shape
    offset = lax.axis_index("rows") * part_width
    bias_first = lax.dynamic_slice_in_dim(bias_one, offset, part_width, 0)
    bias_second = lax.dynamic_slice_in_dim(bias_two, offset, part_width, 0)
    every_row = lax.all_gather(features, "rows", axis=1, tiled=True)
    full_one = norm_silu(every_row, gain_one)
    residual = lax.dynamic_slice_in_dim(every_row, offset, part_width, 3)
    residual = jnp.transpose(residual, (1, 0, 2, 3)).reshape(residual.shape[1], frames, -1)
    conv_one = causal_conv(full_one, weight_one, bias_first).astype(jnp.bfloat16)
    own_rows = own_row(conv_one, frames, columns)
    normed_two = norm_silu(own_rows, gain_two)
    full_two = lax.all_gather(normed_two, "rows", axis=1, tiled=True)
    conv_two = causal_conv(full_two, weight_two, bias_second)
    block_out = (residual.astype(jnp.float32) + conv_two).astype(jnp.bfloat16)
    return own_row(block_out, frames, columns)


def solution(mesh):
    in_specs = (
        P("tm", "rows", None, None),
        P(),
        P("rows", None, None, None, None),
        P(),
        P(),
        P("rows", None, None, None, None),
        P(),
    )
    out_specs = P("tm", "rows", None, None)
    return jax.shard_map(shards, mesh=mesh, in_specs=in_specs, out_specs=out_specs, check_vma=False)
```
